256 devices in a mesh: seq: 16 (over x, y), tp: 16 (over z, core).
Axes of the slice: x: 4, y: 4, z: 8, core: 2. Of those that a mesh axis runs over, the one named last changes fastest.
Arguments:
- query: bfloat16 [16384, 8192], P('seq', 'tp'), may hold values from -6 to 6
- key_in: bfloat16 [16384, 8192], P('seq', 'tp'), may hold values from -6 to 6
- value: bfloat16 [16384, 8192], P('seq', 'tp'), may hold values from -6 to 6
- gate: bfloat16 [16384, 8192], P('seq', 'tp'), may hold values from -8 to 8
- kv_start: float32 [64, 128, 128], P('tp'), may hold values from -240 to 240
- norm_gain: float32 [8192], P('tp'), may hold values from 0.5 to 2
- w_out: bfloat16 [8192, 6144], P('tp'), may hold values from -0.0625 to 0.0625
Outputs:
- mixed: bfloat16 [16384, 6144], P(('seq', 'tp'))
The draws below stay inside these ranges and needn't reach their ends.
All inputs are finite; a program needn't handle non-finite values.
Results may differ from the reference program's by a relative error of at most 0.019.
Values may be sent and summed in bfloat16 or wider, within the bound.
No kernel may reach another device: no remote copies, remote signals or barrier semaphores. Data moves between devices by JAX's collectives and lax.ppermute only.
A program may use at most 128 MiB of HBM per device.

```python
import math
import jax
import jax.numpy as jnp
from jax import lax

D = 6144
H = 64
HD = 128
TOK_DEV = 1024
TOKENS = 16384
N_TP = 16


def level_of(key, extent, split, least, high):
    loudness = 1.0
    for axis_at, parts in split:
        draws = jax.random.uniform(jax.random.fold_in(jax.random.fold_in(key, 6), axis_at), (parts,), jnp.float32, least / len(split), high / len(split))
        loudness = loudness * jnp.repeat(jnp.exp(draws), extent[axis_at] // parts).reshape((-1,) + (1,) * (len(extent) - 1 - axis_at))
    return loudness


def noise(own_key, dims, scale, most, pieces=(), held_as=jnp.bfloat16):
    drawn = jax.random.normal(own_key, dims, jnp.float32) * scale
    if len(pieces) > 0:
        drawn = level_of(own_key, dims, pieces, -0.22, 0.18) * drawn
    return jnp.clip(drawn, min=-most, max=most).astype(held_as)


def setup_inputs(seed: int = 0) -> dict:
    splits = jax.random.split(jax.random.key(seed), 8)
    query = noise(splits[0], (TOKENS, H * HD), 1.0, 6.0, ((0, 16), (1, 16)))
    key_in = noise(splits[1], (TOKENS, H * HD), 1.0, 6.0, ((0, 16), (1, 16)))
    value = noise(splits[2], (TOKENS, H * HD), 1.0, 6.0, ((0, 16), (1, 16)))
    gate = noise(splits[3], (TOKENS, H * HD), 1.5, 8.0, ((0, 16), (1, 16)))
    kv_start = noise(splits[4], (H, HD, HD), 40.0, 240.0, ((0, 16),), jnp.float32)
    norm_gain = jnp.clip(jnp.exp(math.log(2.0) - 1.3862944 * jax.random.uniform(splits[5], (H * HD,), jnp.float32) ** level_of(splits[5], (H * HD,), ((0, 16),), -0.2, 0.2)), 0.5, 2.0)
    w_out = noise(splits[6], (H * HD, D), (H * HD) ** -0.5, 0.0625, ((0, 16),))
    return dict(query=query, key_in=key_in, value=value, gate=gate, kv_start=kv_start, norm_gain=norm_gain, w_out=w_out)


def reference(query, key_in, value, gate, kv_start, norm_gain, w_out):
    block = min(512, TOK_DEV)
    count = TOKENS // block
    highest = lax.Precision.HIGHEST

    def step(state, index):
        start = (index * block).astype(jnp.int32)
        q_blk = lax.dynamic_slice_in_dim(query, start, block, 0).astype(jnp.float32)
        k_blk = lax.dynamic_slice_in_dim(key_in, start, block, 0).astype(jnp.float32)
        v_blk = lax.dynamic_slice_in_dim(value, start, block, 0)
        qa = jax.nn.silu(q_blk).astype(jnp.bfloat16).reshape(block, H, HD).astype(jnp.float32)
        ka = jax.nn.silu(k_blk).astype(jnp.bfloat16).reshape(block, H, HD).astype(jnp.float32)
        va = v_blk.reshape(block, H, HD).astype(jnp.float32)
        inter = jnp.einsum('thd,hde->the', qa, state, precision=highest)
        scores = jnp.einsum('thd,shd->hts', qa, ka, precision=highest)
        causal = jnp.arange(block)[:, None] >= jnp.arange(block)[None, :]
        scores = jnp.where(causal[None], scores, jnp.float32(0.0))
        intra = jnp.einsum('hts,she->the', scores, va, precision=highest)
        new_state = state + jnp.einsum('thd,the->hde', ka, va, precision=highest)
        return (new_state, inter + intra)
    _, outputs = lax.scan(step, kv_start.astype(jnp.float32), jnp.arange(count))
    heads_out = outputs.reshape(TOKENS, H, HD)
    scale = lax.rsqrt(lax.optimization_barrier(jnp.mean(heads_out * heads_out, axis=-1, keepdims=True)) + 1e-05)
    normed = (heads_out * scale).reshape(TOKENS, H * HD)
    attn = (normed * norm_gain[None, :] * jax.nn.sigmoid(gate.astype(jnp.float32))).astype(jnp.bfloat16)
    width = H * HD // N_TP
    total = jnp.zeros((TOKENS, D), jnp.float32)
    for group in range(N_TP):
        part = jnp.dot(attn[:, group * width:(group + 1) * width], w_out[group * width:(group + 1) * width], preferred_element_type=jnp.float32)
        total = total + part.astype(jnp.bfloat16).astype(jnp.float32)
    return total.astype(jnp.bfloat16)
```

```python
import jax
import jax.numpy as jnp
from jax import lax
from jax.sharding import PartitionSpec as P

HD = 128


def row_length(n):
    best = 1
    for r in range(1, n + 1):
        if n % r == 0 and r * r <= n:
            best = r
    return best


def exclusive_prefix(total):
    n = lax.axis_size("seq")
    r = row_length(n)
    rows = n // r
    index = lax.axis_index("seq")
    along = index % r
    sent = total.astype(jnp.bfloat16)
    row_total = sent.astype(jnp.float32)
    before = jnp.zeros_like(row_total)
    for k in range(1, r):
        perm = [(a * r + b, a * r + (b + k) % r) for a in range(rows) for b in range(r)]
        got = lax.ppermute(sent, "seq", perm).astype(jnp.float32)
        row_total = row_total + got
        before = before + jnp.where(k <= along, got, jnp.float32(0.0))
    for k in range(1, rows):
        perm = [(a * r + b, (a + k) * r + b) for a in range(rows - k) for b in range(r)]
        before = before + lax.ppermute(row_total, "seq", perm)
    return before


def per_device(query, key_in, value, gate, kv_start, norm_gain, w_out):
    rows = query.shape[0]
    heads = query.shape[1] // HD
    block = min(512, rows)
    count = rows // block
    highest = lax.Precision.HIGHEST
    qa = (
        jax.nn.silu(query.astype(jnp.float32)).astype(jnp.bfloat16).reshape(count, block, heads, HD)
    )
    ka = (
        jax.nn.silu(key_in.astype(jnp.float32))
        .astype(jnp.bfloat16)
        .reshape(count, block, heads, HD)
    )
    va = value.reshape(count, block, heads, HD)
    block_states = jnp.einsum("nthd,nthe->nhde", ka, va, preferred_element_type=jnp.float32)
    own_total = jnp.sum(block_states, axis=0)
    local_before = jnp.cumsum(block_states, axis=0) - block_states
    prior = exclusive_prefix(own_total)
    states = local_before + (kv_start + prior)[None]
    q_float = qa.astype(jnp.float32)
    inter = jnp.einsum("nthd,nhde->nthe", q_float, states, precision=highest)
    scores = jnp.einsum("nthd,nshd->nhts", qa, ka, preferred_element_type=jnp.float32)
    causal = jnp.arange(block)[:, None] >= jnp.arange(block)[None, :]
    scores = jnp.where(causal[None, None], scores, jnp.float32(0.0))
    intra = jnp.einsum("nhts,nshe->nthe", scores, va.astype(jnp.float32), precision=highest)
    heads_out = (inter + intra).reshape(rows, heads, HD)
    scale = lax.rsqrt(jnp.mean(heads_out * heads_out, axis=-1, keepdims=True) + 1e-05)
    normed = (heads_out * scale).reshape(rows, heads * HD)
    attn = (normed * norm_gain[None, :] * jax.nn.sigmoid(gate.astype(jnp.float32))).astype(
        jnp.bfloat16
    )
    return lax.psum_scatter(
        jnp.dot(attn, w_out, preferred_element_type=jnp.float32).astype(jnp.bfloat16),
        "tp",
        scatter_dimension=0,
        tiled=True,
    )


def solution(mesh):
    in_specs = (
        P("seq", "tp"),
        P("seq", "tp"),
        P("seq", "tp"),
        P("seq", "tp"),
        P("tp", None, None),
        P("tp"),
        P("tp", None),
    )
    out_specs = P(("seq", "tp"), None)
    return jax.shard_map(
        per_device, mesh=mesh, in_specs=in_specs, out_specs=out_specs, check_vma=False
    )
```

```python
import jax
import jax.numpy as jnp
from jax import lax
from jax.sharding import PartitionSpec as P

HD = 128
CHUNKS = 4


def row_length(n):
    best = 1
    for r in range(1, n + 1):
        if n % r == 0 and r * r <= n:
            best = r
    return best


def exclusive_prefix(total):
    n = lax.axis_size("seq")
    r = row_length(n)
    rows = n // r
    index = lax.axis_index("seq")
    along = index % r
    sent = total.astype(jnp.bfloat16)
    row_total = sent.astype(jnp.float32)
    before = jnp.zeros_like(row_total)
    for k in range(1, r):
        perm = [(a * r + b, a * r + (b + k) % r) for a in range(rows) for b in range(r)]
        got = lax.ppermute(sent, "seq", perm).astype(jnp.float32)
        row_total = row_total + got
        before = before + jnp.where(k <= along, got, jnp.float32(0.0))
    for k in range(1, rows):
        perm = [(a * r + b, (a + k) * r + b) for a in range(rows - k) for b in range(r)]
        before = before + lax.ppermute(row_total, "seq", perm)
    return before


def per_device(query, key_in, value, gate, kv_start, norm_gain, w_out):
    rows = query.shape[0]
    heads = query.shape[1] // HD
    block = min(512, rows)
    count = rows // block
    highest = lax.Precision.HIGHEST
    qa = (
        jax.nn.silu(query.astype(jnp.float32)).astype(jnp.bfloat16).reshape(count, block, heads, HD)
    )
    ka = (
        jax.nn.silu(key_in.astype(jnp.float32))
        .astype(jnp.bfloat16)
        .reshape(count, block, heads, HD)
    )
    va = value.reshape(count, block, heads, HD)
    block_states = jnp.einsum("nthd,nthe->nhde", ka, va, preferred_element_type=jnp.float32)
    own_total = jnp.sum(block_states, axis=0)
    local_before = jnp.cumsum(block_states, axis=0) - block_states
    prior = exclusive_prefix(own_total)
    states = local_before + (kv_start + prior)[None]
    q_float = qa.astype(jnp.float32)
    inter = jnp.einsum("nthd,nhde->nthe", q_float, states, precision=highest)
    scores = jnp.einsum("nthd,nshd->nhts", qa, ka, preferred_element_type=jnp.float32)
    causal = jnp.arange(block)[:, None] >= jnp.arange(block)[None, :]
    scores = jnp.where(causal[None, None], scores, jnp.float32(0.0))
    intra = jnp.einsum("nhts,nshe->nthe", scores, va.astype(jnp.float32), precision=highest)
    heads_out = (inter + intra).reshape(rows, heads, HD)
    n_tp = lax.axis_size("tp")
    chunks = CHUNKS
    per = rows // n_tp // chunks
    split_heads = heads_out.reshape(n_tp, chunks, per, heads, HD)
    split_gate = gate.reshape(n_tp, chunks, per, heads * HD)
    pieces = []
    for c in range(chunks):
        part_out = split_heads[:, c].reshape(n_tp * per, heads, HD)
        scale = lax.rsqrt(jnp.mean(part_out * part_out, axis=-1, keepdims=True) + 1e-05)
        normed = (part_out * scale).reshape(n_tp * per, heads * HD)
        gate_c = split_gate[:, c].reshape(n_tp * per, heads * HD)
        attn = (normed * norm_gain[None, :] * jax.nn.sigmoid(gate_c.astype(jnp.float32))).astype(
            jnp.bfloat16
        )
        partial = jnp.dot(attn, w_out, preferred_element_type=jnp.float32).astype(jnp.bfloat16)
        pieces.append(lax.psum_scatter(partial, "tp", scatter_dimension=0, tiled=True))
    return jnp.concatenate(pieces, axis=0)


def solution(mesh):
    in_specs = (
        P("seq", "tp"),
        P("seq", "tp"),
        P("seq", "tp"),
        P("seq", "tp"),
        P("tp", None, None),
        P("tp"),
        P("tp", None),
    )
    out_specs = P(("seq", "tp"), None)
    return jax.shard_map(
        per_device, mesh=mesh, in_specs=in_specs, out_specs=out_specs, check_vma=False
    )
```

```python
import jax
import jax.numpy as jnp
from jax import lax
from jax.sharding import PartitionSpec as P

HD = 128


def row_length(n):
    best = 1
    for r in range(1, n + 1):
        if n % r == 0 and r * r <= n:
            best = r
    return best


def exclusive_prefix(total):
    n = lax.axis_size("seq")
    r = row_length(n)
    rows = n // r
    index = lax.axis_index("seq")
    along = index % r
    sent = total.astype(jnp.bfloat16)
    row_total = sent.astype(jnp.float32)
    before = jnp.zeros_like(row_total)
    for k in range(1, r):
        perm = [(a * r + b, a * r + (b + k) % r) for a in range(rows) for b in range(r)]
        got = lax.ppermute(sent, "seq", perm).astype(jnp.float32)
        row_total = row_total + got
        before = before + jnp.where(k <= along, got, jnp.float32(0.0))
    for k in range(1, rows):
        perm = [(a * r + b, (a + k) * r + b) for a in range(rows - k) for b in range(r)]
        before = before + lax.ppermute(row_total, "seq", perm)
    return before


def per_device(query, key_in, value, gate, kv_start, norm_gain, w_out):
    rows = query.shape[0]
    heads = query.shape[1] // HD
    block = min(512, rows)
    count = rows // block
    highest = lax.Precision.HIGHEST
    qa = (
        jax.nn.silu(query.astype(jnp.float32)).astype(jnp.bfloat16).reshape(count, block, heads, HD)
    )
    ka = (
        jax.nn.silu(key_in.astype(jnp.float32))
        .astype(jnp.bfloat16)
        .reshape(count, block, heads, HD)
    )
    va = value.reshape(count, block, heads, HD)
    block_states = jnp.einsum("nthd,nthe->nhde", ka, va, preferred_element_type=jnp.float32)
    own_total = jnp.sum(block_states, axis=0)
    local_before = jnp.cumsum(block_states, axis=0) - block_states
    prior = exclusive_prefix(own_total)
    states = local_before + (kv_start + prior)[None]
    q_float = qa.astype(jnp.float32)
    inter = jnp.einsum("nthd,nhde->nthe", q_float, states, precision=highest)
    scores = jnp.einsum("nthd,nshd->nhts", qa, ka, preferred_element_type=jnp.float32)
    causal = jnp.arange(block)[:, None] >= jnp.arange(block)[None, :]
    scores = jnp.where(causal[None, None], scores, jnp.float32(0.0))
    intra = jnp.einsum("nhts,nshe->nthe", scores, va.astype(jnp.float32), precision=highest)
    heads_out = (inter + intra).reshape(rows, heads, HD)
    scale = lax.rsqrt(jnp.mean(heads_out * heads_out, axis=-1, keepdims=True) + 1e-05)
    normed = (heads_out * scale).reshape(rows, heads * HD)
    attn = (normed * norm_gain[None, :] * jax.nn.sigmoid(gate.astype(jnp.float32))).astype(
        jnp.bfloat16
    )
    core = lax.axis_index("core")
    swap = [(0, 1), (1, 0)]
    width = w_out.shape[1] // 2
    other_w = lax.ppermute(lax.dynamic_slice_in_dim(w_out, (1 - core) * width, width, 1), "core", swap)
    own_w = lax.dynamic_slice_in_dim(w_out, core * width, width, 1)
    other_attn = lax.ppermute(attn, "core", swap)
    partial = jnp.dot(
        jnp.concatenate([attn, other_attn], axis=1),
        jnp.concatenate([own_w, other_w], axis=0),
        preferred_element_type=jnp.float32,
    ).astype(jnp.bfloat16)
    summed = lax.psum_scatter(partial, "z", scatter_dimension=0, tiled=True)
    half = summed.shape[0] // 2
    keep = lax.dynamic_slice_in_dim(summed, core * half, half, 0)
    give = lax.dynamic_slice_in_dim(summed, (1 - core) * half, half, 0)
    got = lax.ppermute(give, "core", swap)
    return jnp.where(core == 0, jnp.concatenate([keep, got], axis=1), jnp.concatenate([got, keep], axis=1))


def solution(mesh):
    n_tp = mesh.shape["tp"]
    devices = mesh.devices.reshape(mesh.shape["seq"], n_tp // 2, 2)
    inner = jax.sharding.Mesh(devices, ("seq", "z", "core"))
    tp = ("z", "core")
    in_specs = (
        P("seq", tp),
        P("seq", tp),
        P("seq", tp),
        P("seq", tp),
        P(tp, None, None),
        P(tp),
        P(tp, None),
    )
    out_specs = P(("seq", "z", "core"), None)
    return jax.shard_map(
        per_device, mesh=inner, in_specs=in_specs, out_specs=out_specs, check_vma=False
    )
```

```python
import jax
import jax.numpy as jnp
from jax import lax
from jax.sharding import PartitionSpec as P

HD = 128


def row_length(n):
    best = 1
    for r in range(1, n + 1):
        if n % r == 0 and r * r <= n:
            best = r
    return best


def exclusive_prefix(total):
    n = lax.axis_size("seq")
    r = row_length(n)
    rows = n // r
    index = lax.axis_index("seq")
    along = index % r
    sent = total.astype(jnp.bfloat16)
    row_total = sent.astype(jnp.float32)
    before = jnp.zeros_like(row_total)
    for k in range(1, r):
        perm = [(a * r + b, a * r + (b + k) % r) for a in range(rows) for b in range(r)]
        got = lax.ppermute(sent, "seq", perm).astype(jnp.float32)
        row_total = row_total + got
        before = before + jnp.where(k <= along, got, jnp.float32(0.0))
    for k in range(1, rows):
        perm = [(a * r + b, (a + k) * r + b) for a in range(rows - k) for b in range(r)]
        before = before + lax.ppermute(row_total, "seq", perm)
    return before


def per_device(query, key_in, value, gate, kv_start, norm_gain, w_out):
    rows = query.shape[0]
    heads = query.shape[1] // HD
    block = min(512, rows)
    count = rows // block
    highest = lax.Precision.HIGHEST
    qa = (
        jax.nn.silu(query.astype(jnp.float32)).astype(jnp.bfloat16).reshape(count, block, heads, HD)
    )
    ka = (
        jax.nn.silu(key_in.astype(jnp.float32))
        .astype(jnp.bfloat16)
        .reshape(count, block, heads, HD)
    )
    va = value.reshape(count, block, heads, HD)
    block_states = jnp.einsum("nthd,nthe->nhde", ka, va, preferred_element_type=jnp.float32)
    own_total = jnp.sum(block_states, axis=0)
    local_before = jnp.cumsum(block_states, axis=0) - block_states
    prior = exclusive_prefix(own_total)
    states = local_before + (kv_start + prior)[None]
    q_float = qa.astype(jnp.float32)
    inter = jnp.einsum("nthd,nhde->nthe", q_float, states, precision=highest)
    scores = jnp.einsum("nthd,nshd->nhts", qa, ka, preferred_element_type=jnp.float32)
    causal = jnp.arange(block)[:, None] >= jnp.arange(block)[None, :]
    scores = jnp.where(causal[None, None], scores, jnp.float32(0.0))
    intra = jnp.einsum("nhts,nshe->nthe", scores, va.astype(jnp.float32), precision=highest)
    heads_out = (inter + intra).reshape(rows, heads, HD)
    scale = lax.rsqrt(jnp.mean(heads_out * heads_out, axis=-1, keepdims=True) + 1e-05)
    normed = (heads_out * scale).reshape(rows, heads * HD)
    attn = (normed * norm_gain[None, :] * jax.nn.sigmoid(gate.astype(jnp.float32))).astype(
        jnp.bfloat16
    )
    return ring_projection(attn, w_out)


def ring_projection(attn, w_out):
    n = lax.axis_size("z")
    z = lax.axis_index("z")
    core = lax.axis_index("core")
    swap = [(0, 1), (1, 0)]
    rows, width = attn.shape
    per = rows // (2 * n)
    other_w = lax.ppermute(w_out, "core", swap)
    both_w = jnp.concatenate([w_out, other_w], axis=0)
    split = attn.reshape(n, 2, per, width)
    mine = lax.dynamic_index_in_dim(split, core, 1, keepdims=False)
    theirs = lax.ppermute(lax.dynamic_index_in_dim(split, 1 - core, 1, keepdims=False), "core", swap)
    both_attn = jnp.concatenate([mine, theirs], axis=-1)
    half = w_out.shape[1] // 2
    w_cw = both_w[:, :half]
    w_ccw = both_w[:, half:]

    def term(block, w):
        a = lax.dynamic_index_in_dim(both_attn, block % n, 0, keepdims=False)
        return jnp.dot(a, w, preferred_element_type=jnp.float32)

    cw = [(j, (j + 1) % n) for j in range(n)]
    ccw = [(j, (j - 1) % n) for j in range(n)]
    acc_cw = term(z + n - 1, w_cw).astype(jnp.bfloat16)
    acc_ccw = term(z + 1, w_ccw).astype(jnp.bfloat16)
    for s in range(n - 1):
        got_cw = lax.ppermute(acc_cw, "z", cw)
        got_ccw = lax.ppermute(acc_ccw, "z", ccw)
        acc_cw = (got_cw.astype(jnp.float32) + term(z + 2 * n - 2 - s, w_cw)).astype(jnp.bfloat16)
        acc_ccw = (got_ccw.astype(jnp.float32) + term(z + 2 + s, w_ccw)).astype(jnp.bfloat16)
    return jnp.concatenate([acc_cw, acc_ccw], axis=1)


def solution(mesh):
    n_tp = mesh.shape["tp"]
    devices = mesh.devices.reshape(mesh.shape["seq"], n_tp // 2, 2)
    inner = jax.sharding.Mesh(devices, ("seq", "z", "core"))
    tp = ("z", "core")
    in_specs = (
        P("seq", tp),
        P("seq", tp),
        P("seq", tp),
        P("seq", tp),
        P(tp, None, None),
        P(tp),
        P(tp, None),
    )
    out_specs = P(("seq", "z", "core"), None)
    return jax.shard_map(
        per_device, mesh=inner, in_specs=in_specs, out_specs=out_specs, check_vma=False
    )
```

```python
import jax
import jax.numpy as jnp
from jax import lax
from jax.sharding import PartitionSpec as P

HD = 128


def row_length(n):
    best = 1
    for r in range(1, n + 1):
        if n % r == 0 and r * r <= n:
            best = r
    return best


def exclusive_prefix(total):
    n = lax.axis_size("seq")
    r = row_length(n)
    rows = n // r
    index = lax.axis_index("seq")
    along = index % r
    sent = total.astype(jnp.bfloat16)
    row_total = sent.astype(jnp.float32)
    before = jnp.zeros_like(row_total)
    for k in range(1, r):
        perm = [(a * r + b, a * r + (b + k) % r) for a in range(rows) for b in range(r)]
        got = lax.ppermute(sent, "seq", perm).astype(jnp.float32)
        row_total = row_total + got
        before = before + jnp.where(k <= along, got, jnp.float32(0.0))
    for k in range(1, rows):
        perm = [(a * r + b, (a + k) * r + b) for a in range(rows - k) for b in range(r)]
        before = before + lax.ppermute(row_total.astype(jnp.bfloat16), "seq", perm).astype(jnp.float32)
    return before


def per_device(query, key_in, value, gate, kv_start, norm_gain, w_out):
    rows = query.shape[0]
    heads = query.shape[1] // HD
    block = min(512, rows)
    count = rows // block
    highest = lax.Precision.HIGHEST
    qa = (
        jax.nn.silu(query.astype(jnp.float32)).astype(jnp.bfloat16).reshape(count, block, heads, HD)
    )
    ka = (
        jax.nn.silu(key_in.astype(jnp.float32))
        .astype(jnp.bfloat16)
        .reshape(count, block, heads, HD)
    )
    va = value.reshape(count, block, heads, HD)
    block_states = jnp.einsum("nthd,nthe->nhde", ka, va, preferred_element_type=jnp.float32)
    own_total = jnp.sum(block_states, axis=0)
    local_before = jnp.cumsum(block_states, axis=0) - block_states
    gated = norm_gain[None, :] * jax.nn.sigmoid(gate.astype(jnp.float32))
    prior = exclusive_prefix(own_total)
    states = local_before + (kv_start + prior)[None]
    q_float = qa.astype(jnp.float32)
    inter = jnp.einsum("nthd,nhde->nthe", q_float, states, precision=highest)
    scores = jnp.einsum("nthd,nshd->nhts", qa, ka, preferred_element_type=jnp.float32)
    causal = jnp.arange(block)[:, None] >= jnp.arange(block)[None, :]
    scores = jnp.where(causal[None, None], scores, jnp.float32(0.0))
    intra = jnp.einsum("nhts,nshe->nthe", scores, va.astype(jnp.float32), precision=highest)
    heads_out = (inter + intra).reshape(rows, heads, HD)
    scale = lax.rsqrt(jnp.mean(heads_out * heads_out, axis=-1, keepdims=True) + 1e-05)
    normed = (heads_out * scale).reshape(rows, heads * HD)
    attn = (normed * gated).astype(jnp.bfloat16)
    attn = lax.optimization_barrier(attn)
    return lax.psum_scatter(
        jnp.dot(attn, w_out, preferred_element_type=jnp.float32).astype(jnp.bfloat16),
        "tp",
        scatter_dimension=0,
        tiled=True,
    )


def solution(mesh):
    in_specs = (
        P("seq", "tp"),
        P("seq", "tp"),
        P("seq", "tp"),
        P("seq", "tp"),
        P("tp", None, None),
        P("tp"),
        P("tp", None),
    )
    out_specs = P(("seq", "tp"), None)
    return jax.shard_map(
        per_device, mesh=mesh, in_specs=in_specs, out_specs=out_specs, check_vma=False
    )
```

```python
import jax
import jax.numpy as jnp
from jax import lax
from jax.sharding import PartitionSpec as P

HD = 128


def row_length(n):
    best = 1
    for r in range(1, n + 1):
        if n % r == 0 and r * r <= n:
            best = r
    return best


def exclusive_prefix(total):
    n = lax.axis_size("seq")
    r = row_length(n)
    rows = n // r
    index = lax.axis_index("seq")
    along = index % r
    sent = total.astype(jnp.bfloat16)
    row_total = sent.astype(jnp.float32)
    before = jnp.zeros_like(row_total)
    for k in range(1, r):
        perm = [(a * r + b, a * r + (b + k) % r) for a in range(rows) for b in range(r)]
        got = lax.ppermute(sent, "seq", perm).astype(jnp.float32)
        row_total = row_total + got
        before = before + jnp.where(k <= along, got, jnp.float32(0.0))
    for k in range(1, rows):
        perm = [(a * r + b, (a + k) * r + b) for a in range(rows - k) for b in range(r)]
        before = before + lax.ppermute(row_total.astype(jnp.bfloat16), "seq", perm).astype(jnp.float32)
    return before


def per_device(query, key_in, value, gate, kv_start, norm_gain, w_out):
    rows = query.shape[0]
    heads = query.shape[1] // HD
    block = min(512, rows)
    count = rows // block
    highest = lax.Precision.HIGH
    qa = (
        jax.nn.silu(query.astype(jnp.float32)).astype(jnp.bfloat16).reshape(count, block, heads, HD)
    )
    ka = (
        jax.nn.silu(key_in.astype(jnp.float32))
        .astype(jnp.bfloat16)
        .reshape(count, block, heads, HD)
    )
    va = value.reshape(count, block, heads, HD)
    block_states = jnp.einsum("nthd,nthe->nhde", ka, va, preferred_element_type=jnp.float32)
    own_total = jnp.sum(block_states, axis=0)
    local_before = jnp.cumsum(block_states, axis=0) - block_states
    gated = norm_gain[None, :] * jax.nn.sigmoid(gate.astype(jnp.float32))
    prior = exclusive_prefix(own_total)
    states = local_before + (kv_start + prior)[None]
    q_float = qa.astype(jnp.float32)
    inter = jnp.einsum("nthd,nhde->nthe", q_float, states, precision=highest)
    scores = jnp.einsum("nthd,nshd->nhts", qa, ka, preferred_element_type=jnp.float32)
    causal = jnp.arange(block)[:, None] >= jnp.arange(block)[None, :]
    scores = jnp.where(causal[None, None], scores, jnp.float32(0.0))
    intra = jnp.einsum("nhts,nshe->nthe", scores, va.astype(jnp.float32), precision=highest)
    heads_out = (inter + intra).reshape(rows, heads, HD)
    scale = lax.rsqrt(jnp.mean(heads_out * heads_out, axis=-1, keepdims=True) + 1e-05)
    normed = (heads_out * scale).reshape(rows, heads * HD)
    attn = (normed * gated).astype(jnp.bfloat16)
    attn = lax.optimization_barrier(attn)
    return lax.psum_scatter(
        jnp.dot(attn, w_out, preferred_element_type=jnp.float32).astype(jnp.bfloat16),
        "tp",
        scatter_dimension=0,
        tiled=True,
    )


def solution(mesh):
    in_specs = (
        P("seq", "tp"),
        P("seq", "tp"),
        P("seq", "tp"),
        P("seq", "tp"),
        P("tp", None, None),
        P("tp"),
        P("tp", None),
    )
    out_specs = P(("seq", "tp"), None)
    return jax.shard_map(
        per_device, mesh=mesh, in_specs=in_specs, out_specs=out_specs, check_vma=False
    )
```

```python
import jax
import jax.numpy as jnp
from jax import lax
from jax.sharding import PartitionSpec as P

HD = 128


def row_length(n):
    best = 1
    for r in range(1, n + 1):
        if n % r == 0 and r * r <= n:
            best = r
    return best


def exclusive_prefix(total):
    n = lax.axis_size("seq")
    r = row_length(n)
    rows = n // r
    index = lax.axis_index("seq")
    along = index % r
    sent = total.astype(jnp.bfloat16)
    row_total = sent.astype(jnp.float32)
    before = jnp.zeros_like(row_total)
    for k in range(1, r):
        perm = [(a * r + b, a * r + (b + k) % r) for a in range(rows) for b in range(r)]
        got = lax.ppermute(sent, "seq", perm).astype(jnp.float32)
        row_total = row_total + got
        before = before + jnp.where(k <= along, got, jnp.float32(0.0))
    for k in range(1, rows):
        perm = [(a * r + b, (a + k) * r + b) for a in range(rows - k) for b in range(r)]
        before = before + lax.ppermute(row_total.astype(jnp.bfloat16), "seq", perm).astype(jnp.float32)
    return before


def per_device(query, key_in, value, gate, kv_start, norm_gain, w_out):
    rows = query.shape[0]
    heads = query.shape[1] // HD
    block = min(512, rows)
    count = rows // block
    high = lax.Precision.HIGH
    qa = jax.nn.silu(query.astype(jnp.float32)).astype(jnp.bfloat16)
    ka = jax.nn.silu(key_in.astype(jnp.float32)).astype(jnp.bfloat16)

    def head(x, h):
        return x[:, h * HD:(h + 1) * HD].reshape(count, block, HD)

    block_states = [
        jnp.einsum("ntd,nte->nde", head(ka, h), head(value, h), preferred_element_type=jnp.float32)
        for h in range(heads)
    ]
    own_total = jnp.stack([jnp.sum(b, axis=0) for b in block_states])
    gated = norm_gain[None, :] * jax.nn.sigmoid(gate.astype(jnp.float32))
    prior = exclusive_prefix(own_total)
    causal = jnp.arange(block)[:, None] >= jnp.arange(block)[None, :]
    normed = []
    for h in range(heads):
        q_h = head(qa, h)
        k_h = head(ka, h)
        v_h = head(value, h)
        states = jnp.cumsum(block_states[h], axis=0) - block_states[h] + (kv_start[h] + prior[h])[None]
        inter = jnp.einsum("ntd,nde->nte", q_h.astype(jnp.float32), states, precision=high)
        scores = jnp.einsum("ntd,nsd->nts", q_h, k_h, preferred_element_type=jnp.float32)
        scores = jnp.where(causal[None], scores, jnp.float32(0.0))
        intra = jnp.einsum("nts,nse->nte", scores, v_h.astype(jnp.float32), precision=high)
        out_h = (inter + intra).reshape(rows, HD)
        scale = lax.rsqrt(jnp.mean(out_h * out_h, axis=-1, keepdims=True) + 1e-05)
        normed.append(out_h * scale)
    attn = (jnp.concatenate(normed, axis=1) * gated).astype(jnp.bfloat16)
    attn = lax.optimization_barrier(attn)
    return lax.psum_scatter(
        jnp.dot(attn, w_out, preferred_element_type=jnp.float32).astype(jnp.bfloat16),
        "tp",
        scatter_dimension=0,
        tiled=True,
    )


def solution(mesh):
    in_specs = (
        P("seq", "tp"),
        P("seq", "tp"),
        P("seq", "tp"),
        P("seq", "tp"),
        P("tp", None, None),
        P("tp"),
        P("tp", None),
    )
    out_specs = P(("seq", "tp"), None)
    return jax.shard_map(
        per_device, mesh=mesh, in_specs=in_specs, out_specs=out_specs, check_vma=False
    )
```

```python
import jax
import jax.numpy as jnp
from jax import lax
from jax.sharding import PartitionSpec as P

HD = 128


def row_length(n):
    best = 1
    for r in range(1, n + 1):
        if n % r == 0 and r * r <= n:
            best = r
    return best


def exclusive_prefix(total):
    n = lax.axis_size("seq")
    r = row_length(n)
    rows = n // r
    index = lax.axis_index("seq")
    along = index % r
    sent = total.astype(jnp.bfloat16)
    row_total = sent.astype(jnp.float32)
    before = jnp.zeros_like(row_total)
    for k in range(1, r):
        perm = [(a * r + b, a * r + (b + k) % r) for a in range(rows) for b in range(r)]
        got = lax.ppermute(sent, "seq", perm).astype(jnp.float32)
        row_total = row_total + got
        before = before + jnp.where(k <= along, got, jnp.float32(0.0))
    for k in range(1, rows):
        perm = [(a * r + b, (a + k) * r + b) for a in range(rows - k) for b in range(r)]
        before = before + lax.ppermute(row_total.astype(jnp.bfloat16), "seq", perm).astype(jnp.float32)
    return before


def per_device(query, key_in, value, gate, kv_start, norm_gain, w_out):
    rows = query.shape[0]
    heads = query.shape[1] // HD
    block = min(512, rows)
    count = rows // block
    high = lax.Precision.HIGH
    qa = jax.nn.silu(query.astype(jnp.float32)).astype(jnp.bfloat16)
    ka = jax.nn.silu(key_in.astype(jnp.float32)).astype(jnp.bfloat16)

    def head(x, h):
        return x[:, h * HD:(h + 1) * HD].reshape(count, block, HD)

    block_states = [
        jnp.einsum("ntd,nte->nde", head(ka, h), head(value, h), preferred_element_type=jnp.float32)
        for h in range(heads)
    ]
    own_total = jnp.stack([jnp.sum(b, axis=0) for b in block_states])
    gated = norm_gain[None, :] * jax.nn.sigmoid(gate.astype(jnp.float32))
    causal = jnp.arange(block)[:, None] >= jnp.arange(block)[None, :]
    early = []
    for h in range(heads):
        q_h = head(qa, h)
        k_h = head(ka, h)
        v_h = head(value, h)
        states = jnp.cumsum(block_states[h], axis=0) - block_states[h] + kv_start[h][None]
        inter = jnp.einsum("ntd,nde->nte", q_h.astype(jnp.float32), states, precision=high)
        scores = jnp.einsum("ntd,nsd->nts", q_h, k_h, preferred_element_type=jnp.float32)
        scores = jnp.where(causal[None], scores, jnp.float32(0.0))
        intra = jnp.einsum("nts,nse->nte", scores, v_h.astype(jnp.float32), precision=high)
        early.append((inter + intra).reshape(rows, HD))
    prior = exclusive_prefix(own_total)
    late = [
        early[h] + jnp.dot(qa[:, h * HD:(h + 1) * HD].astype(jnp.float32), prior[h], precision=high)
        for h in range(heads)
    ]
    out = jnp.concatenate(late, axis=1)
    member = (jnp.arange(heads * HD)[:, None] // HD == jnp.arange(heads)[None, :]).astype(jnp.float32)
    squares = jnp.dot(out * out, member, precision=high)
    scale = lax.rsqrt(squares * (1.0 / HD) + 1e-05)
    attn = (out * jnp.repeat(scale, HD, axis=1) * gated).astype(jnp.bfloat16)
    attn = lax.optimization_barrier(attn)
    return lax.psum_scatter(
        jnp.dot(attn, w_out, preferred_element_type=jnp.float32).astype(jnp.bfloat16),
        "tp",
        scatter_dimension=0,
        tiled=True,
    )


def solution(mesh):
    in_specs = (
        P("seq", "tp"),
        P("seq", "tp"),
        P("seq", "tp"),
        P("seq", "tp"),
        P("tp", None, None),
        P("tp"),
        P("tp", None),
    )
    out_specs = P(("seq", "tp"), None)
    return jax.shard_map(
        per_device, mesh=mesh, in_specs=in_specs, out_specs=out_specs, check_vma=False
    )
```

```python
import jax
import jax.numpy as jnp
from jax import lax
from jax.sharding import PartitionSpec as P

HD = 128


def row_length(n):
    best = 1
    for r in range(1, n + 1):
        if n % r == 0 and r * r <= n:
            best = r
    return best


def exclusive_prefix(total):
    n = lax.axis_size("seq")
    r = row_length(n)
    rows = n // r
    index = lax.axis_index("seq")
    along = index % r
    sent = total.astype(jnp.bfloat16)
    row_total = sent.astype(jnp.float32)
    before = jnp.zeros_like(row_total)
    for k in range(1, r):
        perm = [(a * r + b, a * r + (b + k) % r) for a in range(rows) for b in range(r)]
        got = lax.ppermute(sent, "seq", perm).astype(jnp.float32)
        row_total = row_total + got
        before = before + jnp.where(k <= along, got, jnp.float32(0.0))
    for k in range(1, rows):
        perm = [(a * r + b, (a + k) * r + b) for a in range(rows - k) for b in range(r)]
        before = before + lax.ppermute(row_total.astype(jnp.bfloat16), "seq", perm).astype(jnp.float32)
    return before


def per_device(query, key_in, value, gate, kv_start, norm_gain, w_out):
    rows = query.shape[0]
    heads = query.shape[1] // HD
    block = min(512, rows)
    count = rows // block
    high = lax.Precision.HIGH
    qa = jax.nn.silu(query.astype(jnp.float32)).astype(jnp.bfloat16)
    ka = jax.nn.silu(key_in.astype(jnp.float32)).astype(jnp.bfloat16)

    def head(x, h):
        return x[:, h * HD:(h + 1) * HD].reshape(count, block, HD)

    full_states = jnp.einsum(
        "ntd,nte->nde",
        ka.reshape(count, block, heads * HD),
        value.reshape(count, block, heads * HD),
        preferred_element_type=jnp.float32,
    )
    block_states = [full_states[:, h * HD:(h + 1) * HD, h * HD:(h + 1) * HD] for h in range(heads)]
    own_total = jnp.stack([jnp.sum(b, axis=0) for b in block_states])
    gated = norm_gain[None, :] * jax.nn.sigmoid(gate.astype(jnp.float32))
    prior = exclusive_prefix(own_total)
    causal = jnp.arange(block)[:, None] >= jnp.arange(block)[None, :]
    normed = []
    for h in range(heads):
        q_h = head(qa, h)
        k_h = head(ka, h)
        v_h = head(value, h)
        states = jnp.cumsum(block_states[h], axis=0) - block_states[h] + (kv_start[h] + prior[h])[None]
        inter = jnp.einsum("ntd,nde->nte", q_h.astype(jnp.float32), states, precision=high)
        scores = jnp.einsum("ntd,nsd->nts", q_h, k_h, preferred_element_type=jnp.float32)
        scores = jnp.where(causal[None], scores, jnp.float32(0.0))
        intra = jnp.einsum("nts,nse->nte", scores, v_h.astype(jnp.float32), precision=high)
        out_h = (inter + intra).reshape(rows, HD)
        scale = lax.rsqrt(jnp.mean(out_h * out_h, axis=-1, keepdims=True) + 1e-05)
        normed.append(out_h * scale)
    attn = (jnp.concatenate(normed, axis=1) * gated).astype(jnp.bfloat16)
    attn = lax.optimization_barrier(attn)
    return lax.psum_scatter(
        jnp.dot(attn, w_out, preferred_element_type=jnp.float32).astype(jnp.bfloat16),
        "tp",
        scatter_dimension=0,
        tiled=True,
    )


def solution(mesh):
    in_specs = (
        P("seq", "tp"),
        P("seq", "tp"),
        P("seq", "tp"),
        P("seq", "tp"),
        P("tp", None, None),
        P("tp"),
        P("tp", None),
    )
    out_specs = P(("seq", "tp"), None)
    return jax.shard_map(
        per_device, mesh=mesh, in_specs=in_specs, out_specs=out_specs, check_vma=False
    )
```

```python
import jax
import jax.numpy as jnp
from jax import lax
from jax.sharding import PartitionSpec as P

HD = 128


def row_length(n):
    best = 1
    for r in range(1, n + 1):
        if n % r == 0 and r * r <= n:
            best = r
    return best


def exclusive_prefix(total):
    n = lax.axis_size("seq")
    r = row_length(n)
    rows = n // r
    index = lax.axis_index("seq")
    along = index % r
    sent = total.astype(jnp.bfloat16)
    row_total = sent.astype(jnp.float32)
    before = jnp.zeros_like(row_total)
    for k in range(1, r):
        perm = [(a * r + b, a * r + (b + k) % r) for a in range(rows) for b in range(r)]
        got = lax.ppermute(sent, "seq", perm).astype(jnp.float32)
        row_total = row_total + got
        before = before + jnp.where(k <= along, got, jnp.float32(0.0))
    row = index // r
    for k in range(1, rows):
        perm = [(a * r + b, ((a + k) % rows) * r + b) for a in range(rows) for b in range(r)]
        got = lax.ppermute(row_total.astype(jnp.bfloat16), "seq", perm).astype(jnp.float32)
        before = before + jnp.where(k <= row, got, jnp.float32(0.0))
    return before


def per_device(query, key_in, value, gate, kv_start, norm_gain, w_out):
    rows = query.shape[0]
    heads = query.shape[1] // HD
    block = min(512, rows)
    count = rows // block
    high = lax.Precision.HIGH
    qa = jax.nn.silu(query.astype(jnp.float32)).astype(jnp.bfloat16)
    ka = jax.nn.silu(key_in.astype(jnp.float32)).astype(jnp.bfloat16)

    def head(x, h):
        return x[:, h * HD:(h + 1) * HD].reshape(count, block, HD)

    block_states = [
        jnp.einsum("ntd,nte->nde", head(ka, h), head(value, h), preferred_element_type=jnp.float32)
        for h in range(heads)
    ]
    own_total = jnp.stack([jnp.sum(b, axis=0) for b in block_states])
    gated = norm_gain[None, :] * jax.nn.sigmoid(gate.astype(jnp.float32))
    prior = exclusive_prefix(own_total)
    causal = jnp.arange(block)[:, None] >= jnp.arange(block)[None, :]
    normed = []
    for h in range(heads):
        q_h = head(qa, h)
        k_h = head(ka, h)
        v_h = head(value, h)
        states = jnp.cumsum(block_states[h], axis=0) - block_states[h] + (kv_start[h] + prior[h])[None]
        inter = jnp.einsum("ntd,nde->nte", q_h.astype(jnp.float32), states, precision=high)
        scores = jnp.einsum("ntd,nsd->nts", q_h, k_h, preferred_element_type=jnp.float32)
        scores = jnp.where(causal[None], scores, jnp.float32(0.0))
        intra = jnp.einsum("nts,nse->nte", scores, v_h.astype(jnp.float32), precision=high)
        out_h = (inter + intra).reshape(rows, HD)
        scale = lax.rsqrt(jnp.mean(out_h * out_h, axis=-1, keepdims=True) + 1e-05)
        normed.append(out_h * scale)
    attn = (jnp.concatenate(normed, axis=1) * gated).astype(jnp.bfloat16)
    attn = lax.optimization_barrier(attn)
    return lax.psum_scatter(
        jnp.dot(attn, w_out, preferred_element_type=jnp.float32).astype(jnp.bfloat16),
        "tp",
        scatter_dimension=0,
        tiled=True,
    )


def solution(mesh):
    in_specs = (
        P("seq", "tp"),
        P("seq", "tp"),
        P("seq", "tp"),
        P("seq", "tp"),
        P("tp", None, None),
        P("tp"),
        P("tp", None),
    )
    out_specs = P(("seq", "tp"), None)
    return jax.shard_map(
        per_device, mesh=mesh, in_specs=in_specs, out_specs=out_specs, check_vma=False
    )
```

```python
import jax
import jax.numpy as jnp
from jax import lax
from jax.sharding import PartitionSpec as P

HD = 128


def row_length(n):
    best = 1
    for r in range(1, n + 1):
        if n % r == 0 and r * r <= n:
            best = r
    return best


def exclusive_prefix(total):
    n = lax.axis_size("seq")
    r = row_length(n)
    rows = n // r
    index = lax.axis_index("seq")
    along = index % r
    sent = total.astype(jnp.bfloat16)
    row_total = sent.astype(jnp.float32)
    before = jnp.zeros_like(row_total)
    for k in range(1, r):
        perm = [(a * r + b, a * r + (b + k) % r) for a in range(rows) for b in range(r)]
        got = lax.ppermute(sent, "seq", perm).astype(jnp.float32)
        row_total = row_total + got
        before = before + jnp.where(k <= along, got, jnp.float32(0.0))
    row = index // r
    for k in range(1, rows):
        perm = [(a * r + b, ((a + k) % rows) * r + b) for a in range(rows) for b in range(r)]
        got = lax.ppermute(row_total.astype(jnp.bfloat16), "seq", perm).astype(jnp.float32)
        before = before + jnp.where(k <= row, got, jnp.float32(0.0))
    return before


def per_device(query, key_in, value, gate, kv_start, norm_gain, w_out):
    rows = query.shape[0]
    heads = query.shape[1] // HD
    block = min(512, rows)
    count = rows // block
    high = lax.Precision.HIGH
    qa = jax.nn.silu(query.astype(jnp.float32)).astype(jnp.bfloat16)
    ka = jax.nn.silu(key_in.astype(jnp.float32)).astype(jnp.bfloat16)

    def head(x, h):
        return x[:, h * HD:(h + 1) * HD].reshape(count, block, HD)

    full_states = jnp.einsum(
        "ntd,nte->nde",
        ka.reshape(count, block, heads * HD),
        value.reshape(count, block, heads * HD),
        preferred_element_type=jnp.float32,
    )
    block_states = [full_states[:, h * HD:(h + 1) * HD, h * HD:(h + 1) * HD] for h in range(heads)]
    own_total = jnp.stack([jnp.sum(b, axis=0) for b in block_states])
    gated = norm_gain[None, :] * jax.nn.sigmoid(gate.astype(jnp.float32))
    prior = exclusive_prefix(own_total)
    causal = jnp.arange(block)[:, None] >= jnp.arange(block)[None, :]
    normed = []
    for h in range(heads):
        q_h = head(qa, h)
        k_h = head(ka, h)
        v_h = head(value, h)
        states = jnp.cumsum(block_states[h], axis=0) - block_states[h] + (kv_start[h] + prior[h])[None]
        inter = jnp.einsum("ntd,nde->nte", q_h.astype(jnp.float32), states, precision=high)
        scores = jnp.einsum("ntd,nsd->nts", q_h, k_h, preferred_element_type=jnp.float32)
        scores = jnp.where(causal[None], scores, jnp.float32(0.0))
        intra = jnp.einsum("nts,nse->nte", scores, v_h.astype(jnp.float32), precision=high)
        out_h = (inter + intra).reshape(rows, HD)
        scale = lax.rsqrt(jnp.mean(out_h * out_h, axis=-1, keepdims=True) + 1e-05)
        normed.append(out_h * scale)
    attn = (jnp.concatenate(normed, axis=1) * gated).astype(jnp.bfloat16)
    attn = lax.optimization_barrier(attn)
    return lax.psum_scatter(
        jnp.dot(attn, w_out, preferred_element_type=jnp.float32).astype(jnp.bfloat16),
        "tp",
        scatter_dimension=0,
        tiled=True,
    )


def solution(mesh):
    in_specs = (
        P("seq", "tp"),
        P("seq", "tp"),
        P("seq", "tp"),
        P("seq", "tp"),
        P("tp", None, None),
        P("tp"),
        P("tp", None),
    )
    out_specs = P(("seq", "tp"), None)
    return jax.shard_map(
        per_device, mesh=mesh, in_specs=in_specs, out_specs=out_specs, check_vma=False
    )
```

```python
import jax
import jax.numpy as jnp
from jax import lax
from jax.sharding import PartitionSpec as P

HD = 128


def row_length(n):
    best = 1
    for r in range(1, n + 1):
        if n % r == 0 and r * r <= n:
            best = r
    return best


def exclusive_prefix(total):
    n = lax.axis_size("seq")
    r = row_length(n)
    rows = n // r
    index = lax.axis_index("seq")
    along = index % r
    sent = total.astype(jnp.bfloat16)
    row_total = sent.astype(jnp.float32)
    before = jnp.zeros_like(row_total)
    for k in range(1, r):
        perm = [(a * r + b, a * r + (b + k) % r) for a in range(rows) for b in range(r)]
        got = lax.ppermute(sent, "seq", perm).astype(jnp.float32)
        row_total = row_total + got
        before = before + jnp.where(k <= along, got, jnp.float32(0.0))
    row = index // r
    for k in range(1, rows):
        perm = [(a * r + b, ((a + k) % rows) * r + b) for a in range(rows) for b in range(r)]
        got = lax.ppermute(row_total.astype(jnp.bfloat16), "seq", perm).astype(jnp.float32)
        before = before + jnp.where(k <= row, got, jnp.float32(0.0))
    return before


def per_device(query, key_in, value, gate, kv_start, norm_gain, w_out):
    rows = query.shape[0]
    heads = query.shape[1] // HD
    block = min(512, rows)
    count = rows // block
    high = lax.Precision.HIGH
    qa = jax.nn.silu(query.astype(jnp.float32)).astype(jnp.bfloat16)
    ka = jax.nn.silu(key_in.astype(jnp.float32)).astype(jnp.bfloat16)

    def head(x, h):
        return x[:, h * HD:(h + 1) * HD].reshape(count, block, HD)

    block_states = [
        jnp.einsum("ntd,nte->nde", head(ka, h), head(value, h), preferred_element_type=jnp.float32)
        for h in range(heads)
    ]
    own_total = jnp.stack([jnp.sum(b, axis=0) for b in block_states])
    gated = norm_gain[None, :] * jax.nn.sigmoid(gate.astype(jnp.float32))
    prior = exclusive_prefix(own_total)
    causal = jnp.arange(block)[:, None] >= jnp.arange(block)[None, :]
    normed = []
    for h in range(heads):
        q_h = head(qa, h)
        k_h = head(ka, h)
        v_h = head(value, h)
        states = jnp.cumsum(block_states[h], axis=0) - block_states[h] + (kv_start[h] + prior[h])[None]
        inter = jnp.einsum("ntd,nde->nte", q_h.astype(jnp.float32), states, precision=high)
        scores = jnp.einsum("ntd,nsd->nts", q_h, k_h, preferred_element_type=jnp.float32)
        scores = jnp.where(causal[None], scores, jnp.float32(0.0))
        intra = jnp.einsum("nts,nse->nte", scores, v_h.astype(jnp.float32), precision=high)
        out_h = (inter + intra).reshape(rows, HD)
        squares = jnp.dot(out_h * out_h, jnp.ones((HD, 1), jnp.float32), precision=high)
        scale = lax.rsqrt(squares * (1.0 / HD) + 1e-05)
        normed.append(out_h * scale)
    attn = (jnp.concatenate(normed, axis=1) * gated).astype(jnp.bfloat16)
    attn = lax.optimization_barrier(attn)
    return lax.psum_scatter(
        jnp.dot(attn, w_out, preferred_element_type=jnp.float32).astype(jnp.bfloat16),
        "tp",
        scatter_dimension=0,
        tiled=True,
    )


def solution(mesh):
    in_specs = (
        P("seq", "tp"),
        P("seq", "tp"),
        P("seq", "tp"),
        P("seq", "tp"),
        P("tp", None, None),
        P("tp"),
        P("tp", None),
    )
    out_specs = P(("seq", "tp"), None)
    return jax.shard_map(
        per_device, mesh=mesh, in_specs=in_specs, out_specs=out_specs, check_vma=False
    )
```

```python
import jax
import jax.numpy as jnp
from jax import lax
from jax.sharding import PartitionSpec as P

HD = 128


def row_length(n):
    best = 1
    for r in range(1, n + 1):
        if n % r == 0 and r * r <= n:
            best = r
    return best


def exclusive_prefix(total, start):
    n = lax.axis_size("seq")
    r = row_length(n)
    rows = n // r
    index = lax.axis_index("seq")
    along = index % r
    sent = total.astype(jnp.bfloat16)
    row_total = sent.astype(jnp.float32)
    before = jnp.zeros_like(row_total)
    for k in range(1, r):
        perm = [(a * r + b, a * r + (b + k) % r) for a in range(rows) for b in range(r)]
        got = lax.ppermute(sent, "seq", perm).astype(jnp.float32)
        row_total = row_total + got
        before = before + jnp.where(k <= along, got, jnp.float32(0.0))
    row = index // r
    before = before + start
    for k in range(1, rows):
        perm = [(a * r + b, ((a + k) % rows) * r + b) for a in range(rows) for b in range(r)]
        sent_total = jnp.where(row < rows - k, row_total, jnp.float32(0.0)).astype(jnp.bfloat16)
        before = before + lax.ppermute(sent_total, "seq", perm).astype(jnp.float32)
    return before


def per_device(query, key_in, value, gate, kv_start, norm_gain, w_out):
    rows = query.shape[0]
    heads = query.shape[1] // HD
    block = min(512, rows)
    count = rows // block
    high = lax.Precision.HIGH
    qa = jax.nn.silu(query.astype(jnp.float32)).astype(jnp.bfloat16)
    ka = jax.nn.silu(key_in.astype(jnp.float32)).astype(jnp.bfloat16)

    def head(x, h):
        return x[:, h * HD:(h + 1) * HD].reshape(count, block, HD)

    block_states = [
        jnp.einsum("ntd,nte->nde", head(ka, h), head(value, h), preferred_element_type=jnp.float32)
        for h in range(heads)
    ]
    own_total = jnp.stack([jnp.sum(b, axis=0) for b in block_states])
    gated = norm_gain[None, :] * jax.nn.sigmoid(gate.astype(jnp.float32))
    prior = exclusive_prefix(own_total, kv_start)
    causal = jnp.arange(block)[:, None] >= jnp.arange(block)[None, :]
    normed = []
    for h in range(heads):
        q_h = head(qa, h)
        k_h = head(ka, h)
        v_h = head(value, h)
        states = jnp.cumsum(block_states[h], axis=0) - block_states[h] + prior[h][None]
        inter = jnp.einsum("ntd,nde->nte", q_h.astype(jnp.float32), states, precision=high)
        scores = jnp.einsum("ntd,nsd->nts", q_h, k_h, preferred_element_type=jnp.float32)
        scores = jnp.where(causal[None], scores, jnp.float32(0.0))
        intra = jnp.einsum("nts,nse->nte", scores, v_h.astype(jnp.float32), precision=high)
        out_h = (inter + intra).reshape(rows, HD)
        scale = lax.rsqrt(jnp.mean(out_h * out_h, axis=-1, keepdims=True) + 1e-05)
        normed.append(out_h * scale)
    attn = (jnp.concatenate(normed, axis=1) * gated).astype(jnp.bfloat16)
    attn = lax.optimization_barrier(attn)
    return lax.psum_scatter(
        jnp.dot(attn, w_out, preferred_element_type=jnp.float32).astype(jnp.bfloat16),
        "tp",
        scatter_dimension=0,
        tiled=True,
    )


def solution(mesh):
    in_specs = (
        P("seq", "tp"),
        P("seq", "tp"),
        P("seq", "tp"),
        P("seq", "tp"),
        P("tp", None, None),
        P("tp"),
        P("tp", None),
    )
    out_specs = P(("seq", "tp"), None)
    return jax.shard_map(
        per_device, mesh=mesh, in_specs=in_specs, out_specs=out_specs, check_vma=False
    )
```

```python
import jax
import jax.numpy as jnp
from jax import lax
from jax.sharding import PartitionSpec as P

HD = 128


def row_length(n):
    return n // 2 if n % 2 == 0 else n


def exclusive_prefix(total):
    n = lax.axis_size("seq")
    r = row_length(n)
    rows = n // r
    index = lax.axis_index("seq")
    along = index % r
    sent = total.astype(jnp.bfloat16)
    row_total = sent.astype(jnp.float32)
    before = jnp.zeros_like(row_total)
    for k in range(1, r):
        perm = [(a * r + b, a * r + (b + k) % r) for a in range(rows) for b in range(r)]
        got = lax.ppermute(sent, "seq", perm).astype(jnp.float32)
        row_total = row_total + got
        before = before + jnp.where(k <= along, got, jnp.float32(0.0))
    row = index // r
    for k in range(1, rows):
        perm = [(a * r + b, ((a + k) % rows) * r + b) for a in range(rows) for b in range(r)]
        got = lax.ppermute(row_total.astype(jnp.bfloat16), "seq", perm).astype(jnp.float32)
        before = before + jnp.where(k <= row, got, jnp.float32(0.0))
    return before


def per_device(query, key_in, value, gate, kv_start, norm_gain, w_out):
    rows = query.shape[0]
    heads = query.shape[1] // HD
    block = min(512, rows)
    count = rows // block
    high = lax.Precision.HIGH
    qa = jax.nn.silu(query.astype(jnp.float32)).astype(jnp.bfloat16)
    ka = jax.nn.silu(key_in.astype(jnp.float32)).astype(jnp.bfloat16)

    def head(x, h):
        return x[:, h * HD:(h + 1) * HD].reshape(count, block, HD)

    block_states = [
        jnp.einsum("ntd,nte->nde", head(ka, h), head(value, h), preferred_element_type=jnp.float32)
        for h in range(heads)
    ]
    own_total = jnp.stack([jnp.sum(b, axis=0) for b in block_states])
    gated = norm_gain[None, :] * jax.nn.sigmoid(gate.astype(jnp.float32))
    prior = exclusive_prefix(own_total)
    causal = jnp.arange(block)[:, None] >= jnp.arange(block)[None, :]
    normed = []
    for h in range(heads):
        q_h = head(qa, h)
        k_h = head(ka, h)
        v_h = head(value, h)
        states = jnp.cumsum(block_states[h], axis=0) - block_states[h] + (kv_start[h] + prior[h])[None]
        inter = jnp.einsum("ntd,nde->nte", q_h.astype(jnp.float32), states, precision=high)
        scores = jnp.einsum("ntd,nsd->nts", q_h, k_h, preferred_element_type=jnp.float32)
        scores = jnp.where(causal[None], scores, jnp.float32(0.0))
        intra = jnp.einsum("nts,nse->nte", scores, v_h.astype(jnp.float32), precision=high)
        out_h = (inter + intra).reshape(rows, HD)
        scale = lax.rsqrt(jnp.mean(out_h * out_h, axis=-1, keepdims=True) + 1e-05)
        normed.append(out_h * scale)
    attn = (jnp.concatenate(normed, axis=1) * gated).astype(jnp.bfloat16)
    attn = lax.optimization_barrier(attn)
    return lax.psum_scatter(
        jnp.dot(attn, w_out, preferred_element_type=jnp.float32).astype(jnp.bfloat16),
        "tp",
        scatter_dimension=0,
        tiled=True,
    )


def solution(mesh):
    in_specs = (
        P("seq", "tp"),
        P("seq", "tp"),
        P("seq", "tp"),
        P("seq", "tp"),
        P("tp", None, None),
        P("tp"),
        P("tp", None),
    )
    out_specs = P(("seq", "tp"), None)
    return jax.shard_map(
        per_device, mesh=mesh, in_specs=in_specs, out_specs=out_specs, check_vma=False
    )
```

```python
import jax
import jax.numpy as jnp
from jax import lax
from jax.sharding import PartitionSpec as P

HD = 128


def row_length(n):
    best = 1
    for r in range(1, n + 1):
        if n % r == 0 and r * r <= n:
            best = r
    return best


def exclusive_prefix(total):
    n = lax.axis_size("seq")
    r = row_length(n)
    rows = n // r
    index = lax.axis_index("seq")
    along = index % r
    sent = total.astype(jnp.bfloat16)
    row_total = sent.astype(jnp.float32)
    before = jnp.zeros_like(row_total)
    for k in range(1, r):
        perm = [(a * r + b, a * r + (b + k) % r) for a in range(rows) for b in range(r)]
        got = lax.ppermute(sent, "seq", perm).astype(jnp.float32)
        row_total = row_total + got
        before = before + jnp.where(k <= along, got, jnp.float32(0.0))
    row = index // r
    for k in range(1, rows):
        perm = [(a * r + b, ((a + k) % rows) * r + b) for a in range(rows) for b in range(r)]
        got = lax.ppermute(row_total.astype(jnp.bfloat16), "seq", perm).astype(jnp.float32)
        before = before + jnp.where(k <= row, got, jnp.float32(0.0))
    return before


def per_device(query, key_in, value, gate, kv_start, norm_gain, w_out):
    rows = query.shape[0]
    heads = query.shape[1] // HD
    block = min(512, rows)
    count = rows // block
    high = lax.Precision.HIGH
    qa = jax.nn.silu(query.astype(jnp.float32)).astype(jnp.bfloat16)
    ka = jax.nn.silu(key_in.astype(jnp.float32)).astype(jnp.bfloat16)

    def head(x, h):
        return x[:, h * HD:(h + 1) * HD].reshape(count, block, HD)

    block_states = [
        jnp.einsum("ntd,nte->nde", head(ka, h), head(value, h), preferred_element_type=jnp.float32)
        for h in range(heads)
    ]
    own_total = jnp.stack([jnp.sum(b, axis=0) for b in block_states])
    gated = norm_gain[None, :] * jax.nn.sigmoid(gate.astype(jnp.float32))
    prior = exclusive_prefix(own_total)
    causal = jnp.arange(block)[:, None] >= jnp.arange(block)[None, :]
    normed = []
    for h in range(heads):
        q_h = head(qa, h)
        k_h = head(ka, h)
        v_h = head(value, h)
        states = jnp.cumsum(block_states[h], axis=0) - block_states[h] + (kv_start[h] + prior[h])[None]
        inter = jnp.einsum("ntd,nde->nte", q_h.astype(jnp.float32), states, precision=high)
        scores = jnp.einsum("ntd,nsd->nts", q_h, k_h, preferred_element_type=jnp.float32)
        scores = jnp.where(causal[None], scores, jnp.float32(0.0))
        intra = jnp.einsum("nts,nse->nte", scores, v_h.astype(jnp.float32), precision=high)
        out_h = (inter + intra).reshape(rows, HD)
        scale = lax.rsqrt(jnp.mean(out_h * out_h, axis=-1, keepdims=True) + 1e-05)
        normed.append(out_h * scale)
    attn = (jnp.concatenate(normed, axis=1) * gated).astype(jnp.bfloat16)
    return lax.psum_scatter(
        jnp.dot(attn, w_out, preferred_element_type=jnp.float32).astype(jnp.bfloat16),
        "tp",
        scatter_dimension=0,
        tiled=True,
    )


def solution(mesh):
    in_specs = (
        P("seq", "tp"),
        P("seq", "tp"),
        P("seq", "tp"),
        P("seq", "tp"),
        P("tp", None, None),
        P("tp"),
        P("tp", None),
    )
    out_specs = P(("seq", "tp"), None)
    return jax.shard_map(
        per_device, mesh=mesh, in_specs=in_specs, out_specs=out_specs, check_vma=False
    )
```

```python
import jax
import jax.numpy as jnp
from jax import lax
from jax.sharding import PartitionSpec as P

HD = 128


def row_length(n):
    best = 1
    for r in range(1, n + 1):
        if n % r == 0 and r * r <= n:
            best = r
    return best


def exclusive_prefix(total):
    n = lax.axis_size("seq")
    r = row_length(n)
    rows = n // r
    index = lax.axis_index("seq")
    along = index % r
    sent = total.astype(jnp.bfloat16)
    row_total = sent.astype(jnp.float32)
    before = jnp.zeros_like(row_total)
    for k in range(1, r):
        perm = [(a * r + b, a * r + (b + k) % r) for a in range(rows) for b in range(r)]
        got = lax.ppermute(sent, "seq", perm).astype(jnp.float32)
        row_total = row_total + got
        before = before + jnp.where(k <= along, got, jnp.float32(0.0))
    row = index // r
    for k in range(1, rows):
        perm = [(a * r + b, ((a + k) % rows) * r + b) for a in range(rows) for b in range(r)]
        got = lax.ppermute(row_total.astype(jnp.bfloat16), "seq", perm).astype(jnp.float32)
        before = before + jnp.where(k <= row, got, jnp.float32(0.0))
    return before


def per_device(query, key_in, value, gate, kv_start, norm_gain, w_out):
    rows = query.shape[0]
    heads = query.shape[1] // HD
    block = min(512, rows)
    count = rows // block
    high = lax.Precision.HIGH
    qa = jax.nn.silu(query.astype(jnp.float32)).astype(jnp.bfloat16)
    ka = jax.nn.silu(key_in.astype(jnp.float32)).astype(jnp.bfloat16)

    def head(x, h):
        return x[:, h * HD:(h + 1) * HD].reshape(count, block, HD)

    full_states = jnp.einsum(
        "ntd,nte->nde",
        ka.reshape(count, block, heads * HD),
        value.reshape(count, block, heads * HD),
        preferred_element_type=jnp.float32,
    )
    block_states = [full_states[:, h * HD:(h + 1) * HD, h * HD:(h + 1) * HD] for h in range(heads)]
    own_total = jnp.stack([jnp.sum(b, axis=0) for b in block_states])
    gated = norm_gain[None, :] * jax.nn.sigmoid(gate.astype(jnp.float32))
    prior = exclusive_prefix(own_total)
    causal = jnp.arange(block)[:, None] >= jnp.arange(block)[None, :]
    normed = []
    for h in range(heads):
        q_h = head(qa, h)
        k_h = head(ka, h)
        v_h = head(value, h)
        states = jnp.cumsum(block_states[h], axis=0) - block_states[h] + (kv_start[h] + prior[h])[None]
        inter = jnp.einsum("ntd,nde->nte", q_h.astype(jnp.float32), states, precision=high)
        scores = jnp.einsum("ntd,nsd->nts", q_h, k_h, preferred_element_type=jnp.float32)
        scores = jnp.where(causal[None], scores, jnp.float32(0.0))
        intra = jnp.einsum("nts,nse->nte", scores, v_h.astype(jnp.float32), precision=high)
        out_h = (inter + intra).reshape(rows, HD)
        scale = lax.rsqrt(jnp.mean(out_h * out_h, axis=-1, keepdims=True) + 1e-05)
        normed.append(out_h * scale)
    attn = (jnp.concatenate(normed, axis=1) * gated).astype(jnp.bfloat16)
    return lax.psum_scatter(
        jnp.dot(attn, w_out, preferred_element_type=jnp.float32).astype(jnp.bfloat16),
        "tp",
        scatter_dimension=0,
        tiled=True,
    )


def solution(mesh):
    in_specs = (
        P("seq", "tp"),
        P("seq", "tp"),
        P("seq", "tp"),
        P("seq", "tp"),
        P("tp", None, None),
        P("tp"),
        P("tp", None),
    )
    out_specs = P(("seq", "tp"), None)
    return jax.shard_map(
        per_device, mesh=mesh, in_specs=in_specs, out_specs=out_specs, check_vma=False
    )
```
